512 devices in a mesh: wide: 64 (over x, z), narrow: 8 (over y, core).
Axes of the slice: x: 4, y: 4, z: 16, core: 2. Of those that a mesh axis runs over, the one named last changes fastest.
Arguments:
- tokens: bfloat16 [49152, 2048], P('wide', 'narrow'), may hold values from -6 to 6
- norm_gain: float32 [2048], replicated, may hold values from 0.1 to 1.9
- qkv_weight: bfloat16 [2048, 3, 2048], P('wide', None, 'narrow'), may hold values from -0.125 to 0.125
- out_weight: bfloat16 [2048, 2048], P('wide', 'narrow'), may hold values from -0.25 to 0.25
- cache_pool: bfloat16 [1536, 128, 2, 2048], P('wide', None, None, 'narrow'), may hold values from -400 to 400, as said below
- prefix_pool: bfloat16 [2048, 2, 2048], P('wide', None, 'narrow'), may hold values from -6 to 6
- page_table: int32 [64, 24], P('wide'), may hold values from 0 to 23, each once within a row
- cache_len: int32 [64], P('wide'), may hold values from 512 to 3072
- group_ids: int32 [64], P('wide'), may hold values from 0 to 7, as said below
- group_pages: int32 [16], replicated, may hold values from 0 to 15, each once
Outputs:
- branch_out: bfloat16 [49152, 2048], P('wide', 'narrow')
- new_pages: bfloat16 [49152, 2, 2048], P('wide', None, 'narrow')
The draws below stay inside these ranges and needn't reach their ends.
Inputs may be any that keep to these rules, and one draw needn't show every extreme that they name: `page_table`: each row is a permutation of the 24 pages of that request. `group_ids`: each group has 8 requests. `group_pages`: a permutation of the prefix pool's pages. `cache_pool`: keys are stored already rotated.
All inputs are finite; a program needn't handle non-finite values.
Results may differ from the reference program's by a relative error of at most 0.0095.
The reference program's roundings to bfloat16 on the way count: a program that leaves them out, or rounds other values in their place, can miss the bound.
Values may be sent and summed in bfloat16 or wider, within the bound.
No kernel may reach another device: no remote copies, remote signals or barrier semaphores. Data moves between devices by JAX's collectives and lax.ppermute only.
A program may use at most 128 MiB of HBM per device.

```python
import jax
import jax.numpy as jnp
from jax import lax

D = 2048
HEADS = 32
HEAD_DIM = 64
ROT = 16
SPAN = 768
PAGE = 128
SLOTS = 24
GROUPS = 8
PPAGES = 2
REQS = 64
TOKENS = 49152
PREF_TOK = 2048


def draw_cache_pool(key, part):
    normal_part = jax.random.normal(jax.random.fold_in(key, 11), (REQS, SLOTS, PAGE, 2, D), jnp.float32)
    normal_part = jnp.clip(normal_part, -6.0, 6.0)
    return normal_part.reshape(REQS * SLOTS, PAGE, 2, D).astype(jnp.bfloat16)


def draw_cache_len(key, part):
    shortest = 4 * PAGE
    longest = SLOTS * PAGE
    drawn = jax.random.randint(jax.random.fold_in(key, 21), (REQS,), 0, 1001)
    cubed = drawn * drawn // 1000 * drawn // 1000
    lengths = shortest + cubed * (longest - shortest) // 1000
    chosen_one = jax.random.randint(jax.random.fold_in(key, 22), (), 0, REQS)
    return jnp.where(jnp.arange(REQS) == chosen_one, longest, lengths).astype(jnp.int32)


def draw_group_ids(key, part):
    shuffled = jax.random.permutation(jax.random.fold_in(key, 31), REQS)
    return (shuffled % GROUPS).astype(jnp.int32)


def block_scale(own_key, extent, pieces, least, high):
    def one(axis_at, blocks):
        heights = jax.random.uniform(jax.random.fold_in(jax.random.fold_in(own_key, 6), axis_at), (blocks,), jnp.float32, least / len(pieces), high / len(pieces))
        return jnp.repeat(jnp.exp(heights), extent[axis_at] // blocks).reshape((-1,) + (1,) * (len(extent) - axis_at - 1))

    factor_of = one(*pieces[0])
    for cut in pieces[1:]:
        factor_of = factor_of * one(*cut)
    return factor_of


def gaussian(own_key, shape, spread, bound, cuts=(), kind=jnp.bfloat16):
    array = spread * jax.random.normal(own_key, shape, jnp.float32)
    if cuts:
        array = array * block_scale(own_key, shape, cuts, -0.22, 0.18)
    return jnp.clip(array, -bound, bound).astype(kind)


def setup_inputs(seed: int = 0) -> dict:
    streams_of = jax.random.split(jax.random.key(seed), 11)
    tokens = gaussian(streams_of[0], (TOKENS, D), 1.0, 6.0, ((0, 64), (1, 8)))
    norm_gain = jnp.clip(1.0 + 0.18 * jax.random.normal(streams_of[1], (D,), jnp.float32), 0.1, 1.9)
    qkv_weight = gaussian(streams_of[2], (D, 3, D), D ** -0.5, 0.125, ((0, 64), (2, 8)))
    out_weight = gaussian(streams_of[3], (D, D), (D // 4) ** -0.5, 0.25, ((0, 64), (1, 8)))
    cache_pool = draw_cache_pool(jax.random.fold_in(streams_of[10], 71), 0)
    prefix_pool = gaussian(streams_of[5], (PREF_TOK, 2, D), 1.0, 6.0, ((0, 64), (2, 8)))
    page_table = jax.vmap(lambda own: jax.random.permutation(own, SLOTS))(jax.random.split(streams_of[6], REQS)).reshape((REQS, SLOTS)).astype(jnp.int32)
    cache_len = draw_cache_len(jax.random.fold_in(streams_of[10], 71), 0)
    group_ids = draw_group_ids(jax.random.fold_in(streams_of[10], 71), 0)
    group_pages = jax.random.permutation(streams_of[9], GROUPS * PPAGES).astype(jnp.int32)
    return {"tokens": tokens, "norm_gain": norm_gain, "qkv_weight": qkv_weight, "out_weight": out_weight, "cache_pool": cache_pool, "prefix_pool": prefix_pool, "page_table": page_table, "cache_len": cache_len, "group_ids": group_ids, "group_pages": group_pages}


NEGATIVE = -1e+30

def rotary(vectors, positions):
    half_rot = ROT // 2
    frequency = 10000.0 ** (-(jnp.arange(half_rot, dtype=jnp.float32) * 2.0 / ROT))
    angles = positions.astype(jnp.float32)[:, None] * frequency[None, :]
    cos_part = jnp.concatenate([jnp.cos(angles), jnp.cos(angles)], axis=1)[:, None, :]
    sine_part = jnp.concatenate([jnp.sin(angles), jnp.sin(angles)], axis=1)[:, None, :]
    rotated_in = vectors[..., :ROT]
    turned = jnp.concatenate([-rotated_in[..., half_rot:], rotated_in[..., :half_rot]], axis=-1)
    return jnp.concatenate([rotated_in * cos_part + turned * sine_part, vectors[..., ROT:]], axis=-1)

def reference(tokens, norm_gain, qkv_weight, out_weight, cache_pool, prefix_pool, page_table, cache_len, group_ids, group_pages):
    token_count = tokens.shape[0]
    widened = tokens.astype(jnp.float32)
    row_mean = lax.optimization_barrier(jnp.mean(widened, axis=1, keepdims=True))
    centered = widened - row_mean
    variance = lax.optimization_barrier(jnp.mean(centered * centered, axis=1, keepdims=True))
    normed = (centered * lax.rsqrt(variance + 1e-05) * norm_gain.astype(jnp.float32)).astype(jnp.bfloat16)
    projected = jnp.dot(normed, qkv_weight.reshape(D, 3 * D), preferred_element_type=jnp.float32)
    projected = projected.reshape(token_count, 3, HEADS, HEAD_DIM)
    offset = jnp.arange(SPAN, dtype=jnp.int32)
    positions = (PPAGES * PAGE + cache_len[:, None] + offset[None, :]).reshape(token_count).astype(jnp.int32)
    queries = lax.optimization_barrier(rotary(projected[:, 0], positions).astype(jnp.bfloat16))
    keys = lax.optimization_barrier(rotary(projected[:, 1], positions).astype(jnp.bfloat16))
    values = lax.optimization_barrier(projected[:, 2].astype(jnp.bfloat16))
    new_pages = jnp.stack([keys.reshape(token_count, D), values.reshape(token_count, D)], axis=1)
    pool_pages = cache_pool.reshape(REQS, SLOTS, PAGE, 2, HEADS, HEAD_DIM)
    prefix_pages = prefix_pool.reshape(GROUPS * PPAGES, PAGE, 2, HEADS, HEAD_DIM)
    causal = offset[:, None] >= offset[None, :]
    cache_index = jnp.arange(SLOTS * PAGE, dtype=jnp.int32)

    def one_request(items):
        own_queries, own_keys, own_values, own_pool, page_list, length, my_group = items
        cached = jnp.take(own_pool, page_list, axis=0).reshape(SLOTS * PAGE, 2, HEADS, HEAD_DIM)
        chosen = lax.dynamic_slice_in_dim(group_pages, (my_group * PPAGES).astype(jnp.int32), PPAGES)
        shared = jnp.take(prefix_pages, chosen, axis=0).reshape(PPAGES * PAGE, 2, HEADS, HEAD_DIM)
        all_keys = jnp.concatenate([shared[:, 0], cached[:, 0], own_keys], axis=0).astype(jnp.float32)
        all_values = jnp.concatenate([shared[:, 1], cached[:, 1], own_values], axis=0).astype(jnp.float32)
        key_valid = jnp.concatenate([jnp.ones((SPAN, PPAGES * PAGE), dtype=bool), jnp.broadcast_to((cache_index < length)[None, :], (SPAN, SLOTS * PAGE)), causal], axis=1)
        scores = jnp.einsum('qhd,khd->hqk', own_queries.astype(jnp.float32), all_keys) * 0.125
        scores = jnp.where(key_valid[None], scores, NEGATIVE)
        row_max = lax.optimization_barrier(jnp.max(scores, axis=2, keepdims=True))
        expo = jnp.where(key_valid[None], jnp.exp(scores - row_max), 0.0)
        denominator = lax.optimization_barrier(jnp.sum(expo, axis=2))
        probs = lax.optimization_barrier(expo.astype(jnp.bfloat16))
        weighted = jnp.einsum('hqk,khd->qhd', probs.astype(jnp.float32), all_values)
        return (weighted / jnp.transpose(denominator)[:, :, None]).astype(jnp.bfloat16)
    attended = lax.map(one_request, (queries.reshape(REQS, SPAN, HEADS, HEAD_DIM), keys.reshape(REQS, SPAN, HEADS, HEAD_DIM), values.reshape(REQS, SPAN, HEADS, HEAD_DIM), pool_pages, page_table, cache_len, group_ids))
    attended = attended.reshape(token_count, D)
    branch_out = jnp.dot(attended, out_weight, preferred_element_type=jnp.float32).astype(jnp.bfloat16)
    return (branch_out, new_pages)
```

```python
import jax
import jax.numpy as jnp
from jax import lax
from jax.sharding import Mesh, PartitionSpec as P

HEAD_DIM = 64
ROT = 16
PAGE = 128
KB = 4
PPAGES = 2


NEGATIVE = -1e30


def rotary(vectors, positions):
    half_rot = ROT // 2
    frequency = 10000.0 ** (-(jnp.arange(half_rot, dtype=jnp.float32) * 2.0 / ROT))
    angles = positions.astype(jnp.float32)[:, None] * frequency[None, :]
    cos_part = jnp.concatenate([jnp.cos(angles), jnp.cos(angles)], axis=1)[:, None, :]
    sine_part = jnp.concatenate([jnp.sin(angles), jnp.sin(angles)], axis=1)[:, None, :]
    rotated_in = vectors[..., :ROT]
    turned = jnp.concatenate([-rotated_in[..., half_rot:], rotated_in[..., :half_rot]], axis=-1)
    return jnp.concatenate(
        [rotated_in * cos_part + turned * sine_part, vectors[..., ROT:]], axis=-1
    )


def attend(running, queries, keys, values, key_valid):
    row_max, weight_sum, weighted = running
    scores = jnp.einsum("qhd,khd->hqk", queries, keys, preferred_element_type=jnp.float32) * 0.125
    scores = jnp.where(key_valid[None], scores, NEGATIVE)
    new_max = jnp.maximum(row_max, jnp.max(scores, axis=2))
    expo = jnp.where(key_valid[None], jnp.exp(scores - new_max[:, :, None]), 0.0)
    factor = jnp.exp(row_max - new_max)
    weight_sum = weight_sum * factor + jnp.sum(expo, axis=2)
    update = jnp.einsum(
        "hqk,khd->qhd", expo.astype(jnp.bfloat16), values, preferred_element_type=jnp.float32
    )
    weighted = weighted * jnp.transpose(factor)[:, :, None] + update
    return (new_max, weight_sum, weighted)


def local(
    tokens,
    norm_gain,
    qkv_weight,
    out_weight,
    cache_pool,
    prefix_pool,
    page_table,
    cache_len,
    group_ids,
    group_pages,
):
    span_rows = tokens.shape[0]
    local_width = qkv_weight.shape[2]
    heads_here = local_width // HEAD_DIM
    gathered = lax.all_gather(tokens, "narrow", axis=1, tiled=True)
    widened = gathered.astype(jnp.float32)
    row_mean = jnp.mean(widened, axis=1, keepdims=True)
    centered = widened - row_mean
    variance = jnp.mean(centered * centered, axis=1, keepdims=True)
    normed = (centered * lax.rsqrt(variance + 1e-05) * norm_gain).astype(jnp.bfloat16)
    shard_rows = qkv_weight.shape[0]
    merged = jnp.concatenate(
        [
            qkv_weight.reshape(shard_rows, 3 * local_width),
            out_weight,
            prefix_pool.reshape(shard_rows, 2 * local_width),
        ],
        axis=1,
    )
    by_x = lax.all_gather(merged, "wx", axis=0, tiled=False)
    by_xz = lax.all_gather(by_x, "wz", axis=0, tiled=False)
    merged_whole = jnp.transpose(by_xz, (1, 0, 2, 3)).reshape(-1, merged.shape[1])
    piece_rows = merged_whole[:, : 3 * local_width]
    out_rows = merged_whole[:, 3 * local_width : 4 * local_width]
    prefix_whole = merged_whole[:, 4 * local_width :]
    piece_count = piece_rows.shape[0]
    columns = normed
    projected = jnp.dot(
        columns,
        piece_rows.reshape(piece_count, 3 * local_width),
        preferred_element_type=jnp.float32,
    )
    projected = projected.reshape(span_rows, 3, heads_here, HEAD_DIM)
    length = cache_len[0]
    offset = jnp.arange(span_rows, dtype=jnp.int32)
    positions = PPAGES * PAGE + length + offset
    queries = rotary(projected[:, 0], positions).astype(jnp.bfloat16)
    keys = rotary(projected[:, 1], positions).astype(jnp.bfloat16)
    values = projected[:, 2].astype(jnp.bfloat16)
    new_pages = jnp.stack(
        [keys.reshape(span_rows, local_width), values.reshape(span_rows, local_width)], axis=1
    )
    initial = (
        jnp.full((heads_here, span_rows), NEGATIVE, jnp.float32),
        jnp.zeros((heads_here, span_rows), jnp.float32),
        jnp.zeros((span_rows, heads_here, HEAD_DIM), jnp.float32),
    )
    running = attend(initial, queries, keys, values, offset[:, None] >= offset[None, :])
    my_group = group_ids[0]
    prefix_pages = prefix_whole.reshape(-1, PAGE, 2, heads_here, HEAD_DIM)
    chosen = lax.dynamic_slice_in_dim(group_pages, my_group * PPAGES, PPAGES)
    key_rows = jnp.take(prefix_pages, chosen, axis=0).reshape(
        PPAGES * PAGE, 2, heads_here, HEAD_DIM
    )
    running = attend(
        running,
        queries,
        key_rows[:, 0],
        key_rows[:, 1],
        jnp.ones((span_rows, PPAGES * PAGE), dtype=bool),
    )
    page_list = page_table[0]
    block_keys = KB * PAGE
    blocks = (length + block_keys - 1) // block_keys
    key_offset = jnp.arange(block_keys, dtype=jnp.int32)

    def cache_block(block_index, state_now):
        page_ids = lax.dynamic_slice_in_dim(page_list, block_index * KB, KB)
        key_rows = jnp.take(cache_pool, page_ids, axis=0).reshape(
            block_keys, 2, heads_here, HEAD_DIM
        )
        key_valid = jnp.broadcast_to(
            (block_index * block_keys + key_offset < length)[None, :], (span_rows, block_keys)
        )
        return attend(state_now, queries, key_rows[:, 0], key_rows[:, 1], key_valid)

    running = lax.fori_loop(0, blocks, cache_block, running)
    head_values = (
        (running[2] / jnp.transpose(running[1])[:, :, None])
        .astype(jnp.bfloat16)
        .reshape(span_rows, local_width)
    )
    all_heads = lax.all_gather(head_values, "narrow", axis=1, tiled=True)
    columns = all_heads
    branch_out = jnp.dot(
        columns,
        out_rows,
        preferred_element_type=jnp.float32,
    )
    return (branch_out.astype(jnp.bfloat16), new_pages)


def split_mesh(mesh):
    grid = mesh.devices
    try:
        along_x = len({device.coords[0] for device in grid[:, 0]})
    except (AttributeError, TypeError):
        along_x = 4
    shape = (along_x, grid.shape[0] // along_x, grid.shape[1])
    return Mesh(grid.reshape(shape), ("wx", "wz", "narrow"))


def solution(mesh):
    W = ("wx", "wz")
    placed = (
        P(W, "narrow"),
        P(),
        P(W, None, "narrow"),
        P(W, "narrow"),
        P(W, None, None, "narrow"),
        P(W, None, "narrow"),
        P(W, None),
        P(W),
        P(W),
        P(),
    )
    return jax.shard_map(
        local,
        mesh=split_mesh(mesh),
        in_specs=placed,
        out_specs=(P(W, "narrow"), P(W, None, "narrow")),
        check_vma=False,
    )
```

```python
import jax
import jax.numpy as jnp
from jax import lax
from jax.sharding import Mesh, PartitionSpec as P

HEAD_DIM = 64
ROT = 16
PAGE = 128
KB = 4
PPAGES = 2


NEGATIVE = -1e30


def rotary(vectors, positions):
    half_rot = ROT // 2
    frequency = 10000.0 ** (-(jnp.arange(half_rot, dtype=jnp.float32) * 2.0 / ROT))
    angles = positions.astype(jnp.float32)[:, None] * frequency[None, :]
    cos_part = jnp.concatenate([jnp.cos(angles), jnp.cos(angles)], axis=1)[:, None, :]
    sine_part = jnp.concatenate([jnp.sin(angles), jnp.sin(angles)], axis=1)[:, None, :]
    rotated_in = vectors[..., :ROT]
    turned = jnp.concatenate([-rotated_in[..., half_rot:], rotated_in[..., :half_rot]], axis=-1)
    return jnp.concatenate(
        [rotated_in * cos_part + turned * sine_part, vectors[..., ROT:]], axis=-1
    )


def attend(running, queries, keys, values, key_valid):
    row_max, weight_sum, weighted = running
    scores = jnp.einsum("qhd,khd->hqk", queries, keys, preferred_element_type=jnp.float32) * 0.125
    scores = jnp.where(key_valid[None], scores, NEGATIVE)
    new_max = jnp.maximum(row_max, jnp.max(scores, axis=2))
    expo = jnp.where(key_valid[None], jnp.exp(scores - new_max[:, :, None]), 0.0)
    factor = jnp.exp(row_max - new_max)
    weight_sum = weight_sum * factor + jnp.sum(expo, axis=2)
    update = jnp.einsum(
        "hqk,khd->qhd", expo.astype(jnp.bfloat16), values, preferred_element_type=jnp.float32
    )
    weighted = weighted * jnp.transpose(factor)[:, :, None] + update
    return (new_max, weight_sum, weighted)


def local(
    tokens,
    norm_gain,
    qkv_weight,
    out_weight,
    cache_pool,
    prefix_pool,
    page_table,
    cache_len,
    group_ids,
    group_pages,
):
    span_rows = tokens.shape[0]
    local_width = qkv_weight.shape[2]
    heads_here = local_width // HEAD_DIM
    gathered = lax.all_gather(tokens, "narrow", axis=1, tiled=True)
    widened = gathered.astype(jnp.float32)
    row_mean = jnp.mean(widened, axis=1, keepdims=True)
    centered = widened - row_mean
    variance = jnp.mean(centered * centered, axis=1, keepdims=True)
    normed = (centered * lax.rsqrt(variance + 1e-05) * norm_gain).astype(jnp.bfloat16)
    shard_rows = qkv_weight.shape[0]
    merged = jnp.concatenate(
        [
            qkv_weight.reshape(shard_rows, 3 * local_width),
            out_weight,
            prefix_pool.reshape(shard_rows, 2 * local_width),
        ],
        axis=1,
    )
    by_x = lax.all_gather(merged, "wx", axis=0, tiled=False)
    by_xz = lax.all_gather(by_x, "wz", axis=0, tiled=False)
    merged_whole = jnp.transpose(by_xz, (1, 0, 2, 3)).reshape(-1, merged.shape[1])
    piece_rows = merged_whole[:, : 3 * local_width]
    out_rows = merged_whole[:, 3 * local_width : 4 * local_width]
    prefix_whole = merged_whole[:, 4 * local_width :]
    piece_count = piece_rows.shape[0]
    columns = normed
    projected = jnp.dot(
        columns,
        piece_rows.reshape(piece_count, 3 * local_width),
        preferred_element_type=jnp.float32,
    )
    projected = projected.reshape(span_rows, 3, heads_here, HEAD_DIM)
    length = cache_len[0]
    offset = jnp.arange(span_rows, dtype=jnp.int32)
    positions = PPAGES * PAGE + length + offset
    queries = rotary(projected[:, 0], positions).astype(jnp.bfloat16)
    keys = rotary(projected[:, 1], positions).astype(jnp.bfloat16)
    values = projected[:, 2].astype(jnp.bfloat16)
    new_pages = jnp.stack(
        [keys.reshape(span_rows, local_width), values.reshape(span_rows, local_width)], axis=1
    )
    initial = (
        jnp.full((heads_here, span_rows), NEGATIVE, jnp.float32),
        jnp.zeros((heads_here, span_rows), jnp.float32),
        jnp.zeros((span_rows, heads_here, HEAD_DIM), jnp.float32),
    )
    running = attend(initial, queries, keys, values, offset[:, None] >= offset[None, :])
    my_group = group_ids[0]
    prefix_pages = prefix_whole.reshape(-1, PAGE, 2, heads_here, HEAD_DIM)
    chosen = lax.dynamic_slice_in_dim(group_pages, my_group * PPAGES, PPAGES)
    key_rows = jnp.take(prefix_pages, chosen, axis=0).reshape(
        PPAGES * PAGE, 2, heads_here, HEAD_DIM
    )
    running = attend(
        running,
        queries,
        key_rows[:, 0],
        key_rows[:, 1],
        jnp.ones((span_rows, PPAGES * PAGE), dtype=bool),
    )
    page_list = page_table[0]
    page_count = cache_pool.shape[0]
    slot_of_page = (
        jnp.zeros((page_count,), jnp.int32)
        .at[page_list]
        .set(jnp.arange(page_count, dtype=jnp.int32))
    )
    block_keys = KB * PAGE
    key_offset = jnp.arange(block_keys, dtype=jnp.int32)

    def cache_block(block_index, state_now):
        key_rows = lax.dynamic_slice_in_dim(cache_pool, block_index * KB, KB, axis=0).reshape(
            block_keys, 2, heads_here, HEAD_DIM
        )
        slots = lax.dynamic_slice_in_dim(slot_of_page, block_index * KB, KB)
        key_slot = jnp.repeat(slots, PAGE) * PAGE + key_offset % PAGE
        key_valid = jnp.broadcast_to((key_slot < length)[None, :], (span_rows, block_keys))
        return attend(state_now, queries, key_rows[:, 0], key_rows[:, 1], key_valid)

    running = lax.fori_loop(0, page_count // KB, cache_block, running)
    head_values = (
        (running[2] / jnp.transpose(running[1])[:, :, None])
        .astype(jnp.bfloat16)
        .reshape(span_rows, local_width)
    )
    all_heads = lax.all_gather(head_values, "narrow", axis=1, tiled=True)
    columns = all_heads
    branch_out = jnp.dot(
        columns,
        out_rows,
        preferred_element_type=jnp.float32,
    )
    return (branch_out.astype(jnp.bfloat16), new_pages)


def split_mesh(mesh):
    grid = mesh.devices
    try:
        along_x = len({device.coords[0] for device in grid[:, 0]})
    except (AttributeError, TypeError):
        along_x = 4
    shape = (along_x, grid.shape[0] // along_x, grid.shape[1])
    return Mesh(grid.reshape(shape), ("wx", "wz", "narrow"))


def solution(mesh):
    W = ("wx", "wz")
    placed = (
        P(W, "narrow"),
        P(),
        P(W, None, "narrow"),
        P(W, "narrow"),
        P(W, None, None, "narrow"),
        P(W, None, "narrow"),
        P(W, None),
        P(W),
        P(W),
        P(),
    )
    return jax.shard_map(
        local,
        mesh=split_mesh(mesh),
        in_specs=placed,
        out_specs=(P(W, "narrow"), P(W, None, "narrow")),
        check_vma=False,
    )
```

```python
import jax
import jax.numpy as jnp
from jax import lax
from jax.sharding import Mesh, PartitionSpec as P

HEAD_DIM = 64
ROT = 16
PAGE = 128
KB = 4
PPAGES = 2


NEGATIVE = -1e30


def rotary(vectors, positions):
    half_rot = ROT // 2
    frequency = 10000.0 ** (-(jnp.arange(half_rot, dtype=jnp.float32) * 2.0 / ROT))
    angles = positions.astype(jnp.float32)[:, None] * frequency[None, :]
    cos_part = jnp.concatenate([jnp.cos(angles), jnp.cos(angles)], axis=1)[:, None, :]
    sine_part = jnp.concatenate([jnp.sin(angles), jnp.sin(angles)], axis=1)[:, None, :]
    rotated_in = vectors[..., :ROT]
    turned = jnp.concatenate([-rotated_in[..., half_rot:], rotated_in[..., :half_rot]], axis=-1)
    return jnp.concatenate(
        [rotated_in * cos_part + turned * sine_part, vectors[..., ROT:]], axis=-1
    )


def attend(running, queries, keys, values, key_valid):
    row_max, weight_sum, weighted = running
    scores = jnp.einsum("qhd,khd->hqk", queries, keys, preferred_element_type=jnp.float32) * 0.125
    scores = jnp.where(key_valid[None], scores, NEGATIVE)
    new_max = jnp.maximum(row_max, jnp.max(scores, axis=2))
    expo = jnp.where(key_valid[None], jnp.exp(scores - new_max[:, :, None]), 0.0)
    factor = jnp.exp(row_max - new_max)
    weight_sum = weight_sum * factor + jnp.sum(expo, axis=2)
    update = jnp.einsum(
        "hqk,khd->qhd", expo.astype(jnp.bfloat16), values, preferred_element_type=jnp.float32
    )
    weighted = weighted * jnp.transpose(factor)[:, :, None] + update
    return (new_max, weight_sum, weighted)


def gather_columns(part):
    count = lax.axis_size("narrow")
    copies = jnp.broadcast_to(part[None], (count,) + part.shape)
    received = lax.all_to_all(copies, "narrow", 0, 0, tiled=False)
    return jnp.transpose(received, (1, 0, 2)).reshape(part.shape[0], count * part.shape[1])


def local(
    tokens,
    norm_gain,
    qkv_weight,
    out_weight,
    cache_pool,
    prefix_pool,
    page_table,
    cache_len,
    group_ids,
    group_pages,
):
    span_rows = tokens.shape[0]
    local_width = qkv_weight.shape[2]
    heads_here = local_width // HEAD_DIM
    gathered = gather_columns(tokens)
    widened = gathered.astype(jnp.float32)
    row_mean = jnp.mean(widened, axis=1, keepdims=True)
    centered = widened - row_mean
    variance = jnp.mean(centered * centered, axis=1, keepdims=True)
    normed = (centered * lax.rsqrt(variance + 1e-05) * norm_gain).astype(jnp.bfloat16)
    shard_rows = qkv_weight.shape[0]
    merged = jnp.concatenate(
        [
            qkv_weight.reshape(shard_rows, 3 * local_width),
            out_weight,
            prefix_pool.reshape(shard_rows, 2 * local_width),
        ],
        axis=1,
    )
    by_x = lax.all_gather(merged, "wx", axis=0, tiled=False)
    by_xz = lax.all_gather(by_x, "wz", axis=0, tiled=False)
    merged_whole = jnp.transpose(by_xz, (1, 0, 2, 3)).reshape(-1, merged.shape[1])
    piece_rows = merged_whole[:, : 3 * local_width]
    out_rows = merged_whole[:, 3 * local_width : 4 * local_width]
    prefix_whole = merged_whole[:, 4 * local_width :]
    piece_count = piece_rows.shape[0]
    columns = normed
    projected = jnp.dot(
        columns,
        piece_rows.reshape(piece_count, 3 * local_width),
        preferred_element_type=jnp.float32,
    )
    projected = projected.reshape(span_rows, 3, heads_here, HEAD_DIM)
    length = cache_len[0]
    offset = jnp.arange(span_rows, dtype=jnp.int32)
    positions = PPAGES * PAGE + length + offset
    queries = rotary(projected[:, 0], positions).astype(jnp.bfloat16)
    keys = rotary(projected[:, 1], positions).astype(jnp.bfloat16)
    values = projected[:, 2].astype(jnp.bfloat16)
    new_pages = jnp.stack(
        [keys.reshape(span_rows, local_width), values.reshape(span_rows, local_width)], axis=1
    )
    initial = (
        jnp.full((heads_here, span_rows), NEGATIVE, jnp.float32),
        jnp.zeros((heads_here, span_rows), jnp.float32),
        jnp.zeros((span_rows, heads_here, HEAD_DIM), jnp.float32),
    )
    running = attend(initial, queries, keys, values, offset[:, None] >= offset[None, :])
    my_group = group_ids[0]
    prefix_pages = prefix_whole.reshape(-1, PAGE, 2, heads_here, HEAD_DIM)
    chosen = lax.dynamic_slice_in_dim(group_pages, my_group * PPAGES, PPAGES)
    key_rows = jnp.take(prefix_pages, chosen, axis=0).reshape(
        PPAGES * PAGE, 2, heads_here, HEAD_DIM
    )
    running = attend(
        running,
        queries,
        key_rows[:, 0],
        key_rows[:, 1],
        jnp.ones((span_rows, PPAGES * PAGE), dtype=bool),
    )
    page_list = page_table[0]
    page_count = cache_pool.shape[0]
    slot_of_page = (
        jnp.zeros((page_count,), jnp.int32)
        .at[page_list]
        .set(jnp.arange(page_count, dtype=jnp.int32))
    )
    block_keys = KB * PAGE
    key_offset = jnp.arange(block_keys, dtype=jnp.int32)

    def cache_block(block_index, state_now):
        key_rows = lax.dynamic_slice_in_dim(cache_pool, block_index * KB, KB, axis=0).reshape(
            block_keys, 2, heads_here, HEAD_DIM
        )
        slots = lax.dynamic_slice_in_dim(slot_of_page, block_index * KB, KB)
        key_slot = jnp.repeat(slots, PAGE) * PAGE + key_offset % PAGE
        key_valid = jnp.broadcast_to((key_slot < length)[None, :], (span_rows, block_keys))
        return attend(state_now, queries, key_rows[:, 0], key_rows[:, 1], key_valid)

    running = lax.fori_loop(0, page_count // KB, cache_block, running)
    head_values = (
        (running[2] / jnp.transpose(running[1])[:, :, None])
        .astype(jnp.bfloat16)
        .reshape(span_rows, local_width)
    )
    all_heads = lax.all_gather(head_values, "narrow", axis=1, tiled=True)
    columns = all_heads
    branch_out = jnp.dot(
        columns,
        out_rows,
        preferred_element_type=jnp.float32,
    )
    return (branch_out.astype(jnp.bfloat16), new_pages)


def split_mesh(mesh):
    grid = mesh.devices
    try:
        along_x = len({device.coords[0] for device in grid[:, 0]})
    except (AttributeError, TypeError):
        along_x = 4
    shape = (along_x, grid.shape[0] // along_x, grid.shape[1])
    return Mesh(grid.reshape(shape), ("wx", "wz", "narrow"))


def solution(mesh):
    W = ("wx", "wz")
    placed = (
        P(W, "narrow"),
        P(),
        P(W, None, "narrow"),
        P(W, "narrow"),
        P(W, None, None, "narrow"),
        P(W, None, "narrow"),
        P(W, None),
        P(W),
        P(W),
        P(),
    )
    return jax.shard_map(
        local,
        mesh=split_mesh(mesh),
        in_specs=placed,
        out_specs=(P(W, "narrow"), P(W, None, "narrow")),
        check_vma=False,
    )
```

```python
import jax
import jax.numpy as jnp
from jax import lax
from jax.sharding import Mesh, PartitionSpec as P

HEAD_DIM = 64
ROT = 16
PAGE = 128
KB = 4
PPAGES = 2


NEGATIVE = -1e30


def rotary(vectors, positions):
    half_rot = ROT // 2
    frequency = 10000.0 ** (-(jnp.arange(half_rot, dtype=jnp.float32) * 2.0 / ROT))
    angles = positions.astype(jnp.float32)[:, None] * frequency[None, :]
    cos_part = jnp.concatenate([jnp.cos(angles), jnp.cos(angles)], axis=1)[:, None, :]
    sine_part = jnp.concatenate([jnp.sin(angles), jnp.sin(angles)], axis=1)[:, None, :]
    rotated_in = vectors[..., :ROT]
    turned = jnp.concatenate([-rotated_in[..., half_rot:], rotated_in[..., :half_rot]], axis=-1)
    return jnp.concatenate(
        [rotated_in * cos_part + turned * sine_part, vectors[..., ROT:]], axis=-1
    )


def attend(running, queries, keys, values, key_valid):
    row_max, weight_sum, weighted = running
    scores = jnp.einsum("qhd,khd->hqk", queries, keys, preferred_element_type=jnp.float32) * 0.125
    scores = jnp.where(key_valid[None], scores, NEGATIVE)
    new_max = jnp.maximum(row_max, jnp.max(scores, axis=2))
    expo = jnp.where(key_valid[None], jnp.exp(scores - new_max[:, :, None]), 0.0)
    factor = jnp.exp(row_max - new_max)
    weight_sum = weight_sum * factor + jnp.sum(expo, axis=2)
    update = jnp.einsum(
        "hqk,khd->qhd", expo.astype(jnp.bfloat16), values, preferred_element_type=jnp.float32
    )
    weighted = weighted * jnp.transpose(factor)[:, :, None] + update
    return (new_max, weight_sum, weighted)


def gather_columns(part):
    count = lax.axis_size("narrow")
    copies = jnp.broadcast_to(part[None], (count,) + part.shape)
    received = lax.all_to_all(copies, "narrow", 0, 0, tiled=False)
    return jnp.transpose(received, (1, 0, 2)).reshape(part.shape[0], count * part.shape[1])


def local(
    tokens,
    norm_gain,
    qkv_weight,
    out_weight,
    cache_pool,
    prefix_pool,
    page_table,
    cache_len,
    group_ids,
    group_pages,
):
    span_rows = tokens.shape[0]
    local_width = qkv_weight.shape[2]
    heads_here = local_width // HEAD_DIM
    gathered = gather_columns(tokens)
    widened = gathered.astype(jnp.float32)
    row_mean = jnp.mean(widened, axis=1, keepdims=True)
    centered = widened - row_mean
    variance = jnp.mean(centered * centered, axis=1, keepdims=True)
    normed = (centered * lax.rsqrt(variance + 1e-05) * norm_gain).astype(jnp.bfloat16)
    shard_rows = qkv_weight.shape[0]
    merged = jnp.concatenate(
        [
            qkv_weight.reshape(shard_rows, 3 * local_width),
            out_weight,
            prefix_pool.reshape(shard_rows, 2 * local_width),
        ],
        axis=1,
    )
    by_x = lax.all_gather(merged, "wx", axis=0, tiled=False)
    stacked = lax.all_gather(by_x, "wz", axis=0, tiled=False)
    along_z, along_x = stacked.shape[0], stacked.shape[1]
    piece_count = along_z * along_x * shard_rows
    piece_rows = stacked[..., : 3 * local_width].reshape(piece_count, 3 * local_width)
    out_rows = jnp.transpose(
        stacked[..., 3 * local_width : 4 * local_width], (1, 0, 2, 3)
    ).reshape(piece_count, local_width)
    columns = jnp.transpose(
        normed.reshape(span_rows, along_x, along_z, shard_rows), (0, 2, 1, 3)
    ).reshape(span_rows, piece_count)
    projected = jnp.dot(
        columns,
        piece_rows.reshape(piece_count, 3 * local_width),
        preferred_element_type=jnp.float32,
    )
    projected = projected.reshape(span_rows, 3, heads_here, HEAD_DIM)
    length = cache_len[0]
    offset = jnp.arange(span_rows, dtype=jnp.int32)
    positions = PPAGES * PAGE + length + offset
    queries = rotary(projected[:, 0], positions).astype(jnp.bfloat16)
    keys = rotary(projected[:, 1], positions).astype(jnp.bfloat16)
    values = projected[:, 2].astype(jnp.bfloat16)
    new_pages = jnp.stack(
        [keys.reshape(span_rows, local_width), values.reshape(span_rows, local_width)], axis=1
    )
    initial = (
        jnp.full((heads_here, span_rows), NEGATIVE, jnp.float32),
        jnp.zeros((heads_here, span_rows), jnp.float32),
        jnp.zeros((span_rows, heads_here, HEAD_DIM), jnp.float32),
    )
    running = attend(initial, queries, keys, values, offset[:, None] >= offset[None, :])
    my_group = group_ids[0]
    chosen = lax.dynamic_slice_in_dim(group_pages, my_group * PPAGES, PPAGES)
    chunks = PAGE // shard_rows
    chunk_ids = (chosen[:, None] * chunks + jnp.arange(chunks, dtype=jnp.int32)[None, :]).reshape(-1)
    key_rows = stacked[chunk_ids % along_z, chunk_ids // along_z][..., 4 * local_width :].reshape(
        PPAGES * PAGE, 2, heads_here, HEAD_DIM
    )
    running = attend(
        running,
        queries,
        key_rows[:, 0],
        key_rows[:, 1],
        jnp.ones((span_rows, PPAGES * PAGE), dtype=bool),
    )
    page_list = page_table[0]
    page_count = cache_pool.shape[0]
    slot_of_page = (
        jnp.zeros((page_count,), jnp.int32)
        .at[page_list]
        .set(jnp.arange(page_count, dtype=jnp.int32))
    )
    block_keys = KB * PAGE
    key_offset = jnp.arange(block_keys, dtype=jnp.int32)

    def cache_block(block_index, state_now):
        key_rows = lax.dynamic_slice_in_dim(cache_pool, block_index * KB, KB, axis=0).reshape(
            block_keys, 2, heads_here, HEAD_DIM
        )
        slots = lax.dynamic_slice_in_dim(slot_of_page, block_index * KB, KB)
        key_slot = jnp.repeat(slots, PAGE) * PAGE + key_offset % PAGE
        key_valid = jnp.broadcast_to((key_slot < length)[None, :], (span_rows, block_keys))
        return attend(state_now, queries, key_rows[:, 0], key_rows[:, 1], key_valid)

    running = lax.fori_loop(0, page_count // KB, cache_block, running)
    head_values = (
        (running[2] / jnp.transpose(running[1])[:, :, None])
        .astype(jnp.bfloat16)
        .reshape(span_rows, local_width)
    )
    all_heads = lax.all_gather(head_values, "narrow", axis=1, tiled=True)
    columns = all_heads
    branch_out = jnp.dot(
        columns,
        out_rows,
        preferred_element_type=jnp.float32,
    )
    return (branch_out.astype(jnp.bfloat16), new_pages)


def split_mesh(mesh):
    grid = mesh.devices
    try:
        along_x = len({device.coords[0] for device in grid[:, 0]})
    except (AttributeError, TypeError):
        along_x = 4
    shape = (along_x, grid.shape[0] // along_x, grid.shape[1])
    return Mesh(grid.reshape(shape), ("wx", "wz", "narrow"))


def solution(mesh):
    W = ("wx", "wz")
    placed = (
        P(W, "narrow"),
        P(),
        P(W, None, "narrow"),
        P(W, "narrow"),
        P(W, None, None, "narrow"),
        P(W, None, "narrow"),
        P(W, None),
        P(W),
        P(W),
        P(),
    )
    return jax.shard_map(
        local,
        mesh=split_mesh(mesh),
        in_specs=placed,
        out_specs=(P(W, "narrow"), P(W, None, "narrow")),
        check_vma=False,
    )
```

```python
import jax
import jax.numpy as jnp
from jax import lax
from jax.experimental import pallas as pl
from jax.experimental.pallas import tpu as pltpu
from jax.sharding import Mesh, PartitionSpec as P

HEAD_DIM = 64
ROT = 16
PAGE = 128
KB = 4
PPAGES = 2


NEGATIVE = -1e30


def rotary(vectors, positions):
    half_rot = ROT // 2
    frequency = 10000.0 ** (-(jnp.arange(half_rot, dtype=jnp.float32) * 2.0 / ROT))
    angles = positions.astype(jnp.float32)[:, None] * frequency[None, :]
    cos_part = jnp.concatenate([jnp.cos(angles), jnp.cos(angles)], axis=1)[:, None, :]
    sine_part = jnp.concatenate([jnp.sin(angles), jnp.sin(angles)], axis=1)[:, None, :]
    rotated_in = vectors[..., :ROT]
    turned = jnp.concatenate([-rotated_in[..., half_rot:], rotated_in[..., :half_rot]], axis=-1)
    return jnp.concatenate(
        [rotated_in * cos_part + turned * sine_part, vectors[..., ROT:]], axis=-1
    )


def attend(running, queries, keys, values, key_valid):
    row_max, weight_sum, weighted = running
    scores = jnp.einsum("qhd,khd->hqk", queries, keys, preferred_element_type=jnp.float32) * 0.125
    scores = jnp.where(key_valid[None], scores, NEGATIVE)
    new_max = jnp.maximum(row_max, jnp.max(scores, axis=2))
    expo = jnp.where(key_valid[None], jnp.exp(scores - new_max[:, :, None]), 0.0)
    factor = jnp.exp(row_max - new_max)
    weight_sum = weight_sum * factor + jnp.sum(expo, axis=2)
    update = jnp.einsum(
        "hqk,khd->qhd", expo.astype(jnp.bfloat16), values, preferred_element_type=jnp.float32
    )
    weighted = weighted * jnp.transpose(factor)[:, :, None] + update
    return (new_max, weight_sum, weighted)


def cache_attention(queries_hm, keys_hm, values_hm, key_valid, block_keys):
    heads, rows, depth = queries_hm.shape
    total_keys = keys_hm.shape[1]
    steps = total_keys // block_keys

    def body(q_ref, k_ref, v_ref, valid_ref, max_out, sum_out, acc_out, max_s, sum_s, acc_s):
        step = pl.program_id(1)

        @pl.when(step == 0)
        def _():
            max_s[...] = jnp.full(max_s.shape, NEGATIVE, jnp.float32)
            sum_s[...] = jnp.zeros(sum_s.shape, jnp.float32)
            acc_s[...] = jnp.zeros(acc_s.shape, jnp.float32)

        q = q_ref[0]
        k = k_ref[0]
        v = v_ref[0]
        valid = valid_ref[...] > 0
        scores = lax.dot_general(q, k, (((1,), (1,)), ((), ())), preferred_element_type=jnp.float32) * 0.125
        scores = jnp.where(valid, scores, NEGATIVE)
        old_max = max_s[...]
        new_max = jnp.maximum(old_max, jnp.max(scores, axis=1, keepdims=True))
        expo = jnp.where(valid, jnp.exp(scores - new_max), 0.0)
        factor = jnp.exp(old_max - new_max)
        sum_s[...] = sum_s[...] * factor + jnp.sum(expo, axis=1, keepdims=True)
        acc_s[...] = acc_s[...] * factor + lax.dot_general(
            expo.astype(jnp.bfloat16), v, (((1,), (0,)), ((), ())), preferred_element_type=jnp.float32
        )
        max_s[...] = new_max

        @pl.when(step == steps - 1)
        def _():
            max_out[0] = max_s[...]
            sum_out[0] = sum_s[...]
            acc_out[0] = acc_s[...]

    return pl.pallas_call(
        body,
        grid=(heads, steps),
        in_specs=[
            pl.BlockSpec((1, rows, depth), lambda h, s: (h, 0, 0)),
            pl.BlockSpec((1, block_keys, depth), lambda h, s: (h, s, 0)),
            pl.BlockSpec((1, block_keys, depth), lambda h, s: (h, s, 0)),
            pl.BlockSpec((1, block_keys), lambda h, s: (0, s)),
        ],
        out_specs=[
            pl.BlockSpec((1, rows, 1), lambda h, s: (h, 0, 0)),
            pl.BlockSpec((1, rows, 1), lambda h, s: (h, 0, 0)),
            pl.BlockSpec((1, rows, depth), lambda h, s: (h, 0, 0)),
        ],
        out_shape=[
            jax.ShapeDtypeStruct((heads, rows, 1), jnp.float32),
            jax.ShapeDtypeStruct((heads, rows, 1), jnp.float32),
            jax.ShapeDtypeStruct((heads, rows, depth), jnp.float32),
        ],
        scratch_shapes=[
            pltpu.VMEM((rows, 1), jnp.float32),
            pltpu.VMEM((rows, 1), jnp.float32),
            pltpu.VMEM((rows, depth), jnp.float32),
        ],
        compiler_params=pltpu.CompilerParams(dimension_semantics=("parallel", "arbitrary")),
    )(queries_hm, keys_hm, values_hm, key_valid)


def gather_columns(part):
    count = lax.axis_size("narrow")
    copies = jnp.broadcast_to(part[None], (count,) + part.shape)
    received = lax.all_to_all(copies, "narrow", 0, 0, tiled=False)
    return jnp.transpose(received, (1, 0, 2)).reshape(part.shape[0], count * part.shape[1])


def local(
    tokens,
    norm_gain,
    qkv_weight,
    out_weight,
    cache_pool,
    prefix_pool,
    page_table,
    cache_len,
    group_ids,
    group_pages,
):
    span_rows = tokens.shape[0]
    local_width = qkv_weight.shape[2]
    heads_here = local_width // HEAD_DIM
    gathered = gather_columns(tokens)
    widened = gathered.astype(jnp.float32)
    row_mean = jnp.mean(widened, axis=1, keepdims=True)
    centered = widened - row_mean
    variance = jnp.mean(centered * centered, axis=1, keepdims=True)
    normed = (centered * lax.rsqrt(variance + 1e-05) * norm_gain).astype(jnp.bfloat16)
    shard_rows = qkv_weight.shape[0]
    merged = jnp.concatenate(
        [
            qkv_weight.reshape(shard_rows, 3 * local_width),
            out_weight,
            prefix_pool.reshape(shard_rows, 2 * local_width),
        ],
        axis=1,
    )
    by_x = lax.all_gather(merged, "wx", axis=0, tiled=False)
    by_xz = lax.all_gather(by_x, "wz", axis=0, tiled=False)
    merged_whole = jnp.transpose(by_xz, (1, 0, 2, 3)).reshape(-1, merged.shape[1])
    piece_rows = merged_whole[:, : 3 * local_width]
    out_rows = merged_whole[:, 3 * local_width : 4 * local_width]
    prefix_whole = merged_whole[:, 4 * local_width :]
    piece_count = piece_rows.shape[0]
    columns = normed
    projected = jnp.dot(
        columns,
        piece_rows.reshape(piece_count, 3 * local_width),
        preferred_element_type=jnp.float32,
    )
    projected = projected.reshape(span_rows, 3, heads_here, HEAD_DIM)
    length = cache_len[0]
    offset = jnp.arange(span_rows, dtype=jnp.int32)
    positions = PPAGES * PAGE + length + offset
    queries = rotary(projected[:, 0], positions).astype(jnp.bfloat16)
    keys = rotary(projected[:, 1], positions).astype(jnp.bfloat16)
    values = projected[:, 2].astype(jnp.bfloat16)
    new_pages = jnp.stack(
        [keys.reshape(span_rows, local_width), values.reshape(span_rows, local_width)], axis=1
    )
    initial = (
        jnp.full((heads_here, span_rows), NEGATIVE, jnp.float32),
        jnp.zeros((heads_here, span_rows), jnp.float32),
        jnp.zeros((span_rows, heads_here, HEAD_DIM), jnp.float32),
    )
    running = attend(initial, queries, keys, values, offset[:, None] >= offset[None, :])
    my_group = group_ids[0]
    prefix_pages = prefix_whole.reshape(-1, PAGE, 2, heads_here, HEAD_DIM)
    chosen = lax.dynamic_slice_in_dim(group_pages, my_group * PPAGES, PPAGES)
    key_rows = jnp.take(prefix_pages, chosen, axis=0).reshape(
        PPAGES * PAGE, 2, heads_here, HEAD_DIM
    )
    running = attend(
        running,
        queries,
        key_rows[:, 0],
        key_rows[:, 1],
        jnp.ones((span_rows, PPAGES * PAGE), dtype=bool),
    )
    page_list = page_table[0]
    page_count = cache_pool.shape[0]
    slot_of_page = (
        jnp.zeros((page_count,), jnp.int32)
        .at[page_list]
        .set(jnp.arange(page_count, dtype=jnp.int32))
    )
    block_keys = KB * PAGE
    key_slot = (slot_of_page[:, None] * PAGE + jnp.arange(PAGE, dtype=jnp.int32)[None, :]).reshape(1, -1)
    key_valid = (key_slot < length).astype(jnp.int32)
    pool_rows = cache_pool.reshape(page_count * PAGE, 2, heads_here, HEAD_DIM)
    cache_max, cache_sum, cache_acc = cache_attention(
        jnp.transpose(queries, (1, 0, 2)),
        jnp.transpose(pool_rows[:, 0], (1, 0, 2)),
        jnp.transpose(pool_rows[:, 1], (1, 0, 2)),
        key_valid,
        block_keys,
    )
    row_max, weight_sum, weighted = running
    cache_max = cache_max[..., 0]
    both_max = jnp.maximum(row_max, cache_max)
    keep = jnp.exp(row_max - both_max)
    take = jnp.exp(cache_max - both_max)
    running = (
        both_max,
        weight_sum * keep + cache_sum[..., 0] * take,
        weighted * jnp.transpose(keep)[:, :, None]
        + jnp.transpose(cache_acc, (1, 0, 2)) * jnp.transpose(take)[:, :, None],
    )
    head_values = (
        (running[2] / jnp.transpose(running[1])[:, :, None])
        .astype(jnp.bfloat16)
        .reshape(span_rows, local_width)
    )
    all_heads = lax.all_gather(head_values, "narrow", axis=1, tiled=True)
    columns = all_heads
    branch_out = jnp.dot(
        columns,
        out_rows,
        preferred_element_type=jnp.float32,
    )
    return (branch_out.astype(jnp.bfloat16), new_pages)


def split_mesh(mesh):
    grid = mesh.devices
    try:
        along_x = len({device.coords[0] for device in grid[:, 0]})
    except (AttributeError, TypeError):
        along_x = 4
    shape = (along_x, grid.shape[0] // along_x, grid.shape[1])
    return Mesh(grid.reshape(shape), ("wx", "wz", "narrow"))


def solution(mesh):
    W = ("wx", "wz")
    placed = (
        P(W, "narrow"),
        P(),
        P(W, None, "narrow"),
        P(W, "narrow"),
        P(W, None, None, "narrow"),
        P(W, None, "narrow"),
        P(W, None),
        P(W),
        P(W),
        P(),
    )
    return jax.shard_map(
        local,
        mesh=split_mesh(mesh),
        in_specs=placed,
        out_specs=(P(W, "narrow"), P(W, None, "narrow")),
        check_vma=False,
    )
```

```python
import jax
import jax.numpy as jnp
from jax import lax
from jax.sharding import Mesh, PartitionSpec as P

HEAD_DIM = 64
ROT = 16
PAGE = 128
KB = 4
PPAGES = 2


NEGATIVE = -1e30


def rotary(vectors, positions):
    half_rot = ROT // 2
    frequency = 10000.0 ** (-(jnp.arange(half_rot, dtype=jnp.float32) * 2.0 / ROT))
    angles = positions.astype(jnp.float32)[:, None] * frequency[None, :]
    cos_part = jnp.concatenate([jnp.cos(angles), jnp.cos(angles)], axis=1)[:, None, :]
    sine_part = jnp.concatenate([jnp.sin(angles), jnp.sin(angles)], axis=1)[:, None, :]
    rotated_in = vectors[..., :ROT]
    turned = jnp.concatenate([-rotated_in[..., half_rot:], rotated_in[..., :half_rot]], axis=-1)
    return jnp.concatenate(
        [rotated_in * cos_part + turned * sine_part, vectors[..., ROT:]], axis=-1
    )


def attend(running, queries, keys, values, key_valid):
    row_max, weight_sum, weighted = running
    scores = jnp.einsum("hqd,hkd->hqk", queries, keys, preferred_element_type=jnp.float32) * 0.125
    scores = jnp.where(key_valid[None], scores, NEGATIVE)
    new_max = jnp.maximum(row_max, jnp.max(scores, axis=2))
    expo = jnp.where(key_valid[None], jnp.exp(scores - new_max[:, :, None]), 0.0)
    factor = jnp.exp(row_max - new_max)
    weight_sum = weight_sum * factor + jnp.sum(expo, axis=2)
    update = jnp.einsum(
        "hqk,hkd->hqd", expo.astype(jnp.bfloat16), values, preferred_element_type=jnp.float32
    )
    weighted = weighted * factor[:, :, None] + update
    return (new_max, weight_sum, weighted)


def gather_columns(part):
    count = lax.axis_size("narrow")
    copies = jnp.broadcast_to(part[None], (count,) + part.shape)
    received = lax.all_to_all(copies, "narrow", 0, 0, tiled=False)
    return jnp.transpose(received, (1, 0, 2)).reshape(part.shape[0], count * part.shape[1])


def local(
    tokens,
    norm_gain,
    qkv_weight,
    out_weight,
    cache_pool,
    prefix_pool,
    page_table,
    cache_len,
    group_ids,
    group_pages,
):
    span_rows = tokens.shape[0]
    local_width = qkv_weight.shape[2]
    heads_here = local_width // HEAD_DIM
    gathered = gather_columns(tokens)
    widened = gathered.astype(jnp.float32)
    row_mean = jnp.mean(widened, axis=1, keepdims=True)
    centered = widened - row_mean
    variance = jnp.mean(centered * centered, axis=1, keepdims=True)
    normed = (centered * lax.rsqrt(variance + 1e-05) * norm_gain).astype(jnp.bfloat16)
    shard_rows = qkv_weight.shape[0]
    merged = jnp.concatenate(
        [
            qkv_weight.reshape(shard_rows, 3 * local_width),
            out_weight,
            prefix_pool.reshape(shard_rows, 2 * local_width),
        ],
        axis=1,
    )
    by_x = lax.all_gather(merged, "wx", axis=0, tiled=False)
    by_xz = lax.all_gather(by_x, "wz", axis=0, tiled=False)
    merged_whole = jnp.transpose(by_xz, (1, 0, 2, 3)).reshape(-1, merged.shape[1])
    piece_rows = merged_whole[:, : 3 * local_width]
    out_rows = merged_whole[:, 3 * local_width : 4 * local_width]
    prefix_whole = merged_whole[:, 4 * local_width :]
    piece_count = piece_rows.shape[0]
    columns = normed
    projected = jnp.dot(
        columns,
        piece_rows.reshape(piece_count, 3 * local_width),
        preferred_element_type=jnp.float32,
    )
    projected = projected.reshape(span_rows, 3, heads_here, HEAD_DIM)
    length = cache_len[0]
    offset = jnp.arange(span_rows, dtype=jnp.int32)
    positions = PPAGES * PAGE + length + offset
    queries = rotary(projected[:, 0], positions).astype(jnp.bfloat16)
    keys = rotary(projected[:, 1], positions).astype(jnp.bfloat16)
    values = projected[:, 2].astype(jnp.bfloat16)
    new_pages = jnp.stack(
        [keys.reshape(span_rows, local_width), values.reshape(span_rows, local_width)], axis=1
    )
    initial = (
        jnp.full((heads_here, span_rows), NEGATIVE, jnp.float32),
        jnp.zeros((heads_here, span_rows), jnp.float32),
        jnp.zeros((heads_here, span_rows, HEAD_DIM), jnp.float32),
    )
    head_major = lambda rows: jnp.transpose(rows, (1, 0, 2))
    queries_hm = head_major(queries)
    running = attend(
        initial, queries_hm, head_major(keys), head_major(values), offset[:, None] >= offset[None, :]
    )
    my_group = group_ids[0]
    prefix_pages = prefix_whole.reshape(-1, PAGE, 2, heads_here, HEAD_DIM)
    chosen = lax.dynamic_slice_in_dim(group_pages, my_group * PPAGES, PPAGES)
    key_rows = jnp.take(prefix_pages, chosen, axis=0).reshape(
        PPAGES * PAGE, 2, heads_here, HEAD_DIM
    )
    running = attend(
        running,
        queries_hm,
        head_major(key_rows[:, 0]),
        head_major(key_rows[:, 1]),
        jnp.ones((span_rows, PPAGES * PAGE), dtype=bool),
    )
    page_list = page_table[0]
    page_count = cache_pool.shape[0]
    slot_of_page = (
        jnp.zeros((page_count,), jnp.int32)
        .at[page_list]
        .set(jnp.arange(page_count, dtype=jnp.int32))
    )
    block_keys = KB * PAGE
    key_offset = jnp.arange(block_keys, dtype=jnp.int32)

    pool_rows = cache_pool.reshape(page_count * PAGE, 2, heads_here, HEAD_DIM)
    pool_keys = head_major(pool_rows[:, 0])
    pool_values = head_major(pool_rows[:, 1])

    def cache_block(block_index, state_now):
        block_keys_hm = lax.dynamic_slice_in_dim(pool_keys, block_index * block_keys, block_keys, axis=1)
        block_values_hm = lax.dynamic_slice_in_dim(pool_values, block_index * block_keys, block_keys, axis=1)
        slots = lax.dynamic_slice_in_dim(slot_of_page, block_index * KB, KB)
        key_slot = jnp.repeat(slots, PAGE) * PAGE + key_offset % PAGE
        key_valid = jnp.broadcast_to((key_slot < length)[None, :], (span_rows, block_keys))
        return attend(state_now, queries_hm, block_keys_hm, block_values_hm, key_valid)

    running = lax.fori_loop(0, page_count // KB, cache_block, running)
    head_values = (
        jnp.transpose(running[2] / running[1][:, :, None], (1, 0, 2))
        .astype(jnp.bfloat16)
        .reshape(span_rows, local_width)
    )
    all_heads = lax.all_gather(head_values, "narrow", axis=1, tiled=True)
    columns = all_heads
    branch_out = jnp.dot(
        columns,
        out_rows,
        preferred_element_type=jnp.float32,
    )
    return (branch_out.astype(jnp.bfloat16), new_pages)


def split_mesh(mesh):
    grid = mesh.devices
    try:
        along_x = len({device.coords[0] for device in grid[:, 0]})
    except (AttributeError, TypeError):
        along_x = 4
    shape = (along_x, grid.shape[0] // along_x, grid.shape[1])
    return Mesh(grid.reshape(shape), ("wx", "wz", "narrow"))


def solution(mesh):
    W = ("wx", "wz")
    placed = (
        P(W, "narrow"),
        P(),
        P(W, None, "narrow"),
        P(W, "narrow"),
        P(W, None, None, "narrow"),
        P(W, None, "narrow"),
        P(W, None),
        P(W),
        P(W),
        P(),
    )
    return jax.shard_map(
        local,
        mesh=split_mesh(mesh),
        in_specs=placed,
        out_specs=(P(W, "narrow"), P(W, None, "narrow")),
        check_vma=False,
    )
```

```python
import jax
import jax.numpy as jnp
from jax import lax
from jax.sharding import Mesh, PartitionSpec as P

HEAD_DIM = 64
ROT = 16
PAGE = 128
KB = 8
PPAGES = 2


NEGATIVE = -1e30


def rotary(vectors, positions):
    half_rot = ROT // 2
    frequency = 10000.0 ** (-(jnp.arange(half_rot, dtype=jnp.float32) * 2.0 / ROT))
    angles = positions.astype(jnp.float32)[:, None] * frequency[None, :]
    cos_part = jnp.concatenate([jnp.cos(angles), jnp.cos(angles)], axis=1)[:, None, :]
    sine_part = jnp.concatenate([jnp.sin(angles), jnp.sin(angles)], axis=1)[:, None, :]
    rotated_in = vectors[..., :ROT]
    turned = jnp.concatenate([-rotated_in[..., half_rot:], rotated_in[..., :half_rot]], axis=-1)
    return jnp.concatenate(
        [rotated_in * cos_part + turned * sine_part, vectors[..., ROT:]], axis=-1
    )


def attend(running, queries, keys, values, key_valid):
    row_max, weight_sum, weighted = running
    scores = jnp.einsum("qhd,khd->hqk", queries, keys, preferred_element_type=jnp.float32) * 0.125
    scores = jnp.where(key_valid[None], scores, NEGATIVE)
    new_max = jnp.maximum(row_max, jnp.max(scores, axis=2))
    expo = jnp.where(key_valid[None], jnp.exp(scores - new_max[:, :, None]), 0.0)
    factor = jnp.exp(row_max - new_max)
    weight_sum = weight_sum * factor + jnp.sum(expo, axis=2)
    update = jnp.einsum(
        "hqk,khd->qhd", expo.astype(jnp.bfloat16), values, preferred_element_type=jnp.float32
    )
    weighted = weighted * jnp.transpose(factor)[:, :, None] + update
    return (new_max, weight_sum, weighted)


def gather_columns(part):
    count = lax.axis_size("narrow")
    copies = jnp.broadcast_to(part[None], (count,) + part.shape)
    received = lax.all_to_all(copies, "narrow", 0, 0, tiled=False)
    return jnp.transpose(received, (1, 0, 2)).reshape(part.shape[0], count * part.shape[1])


def local(
    tokens,
    norm_gain,
    qkv_weight,
    out_weight,
    cache_pool,
    prefix_pool,
    page_table,
    cache_len,
    group_ids,
    group_pages,
):
    span_rows = tokens.shape[0]
    local_width = qkv_weight.shape[2]
    heads_here = local_width // HEAD_DIM
    gathered = gather_columns(tokens)
    widened = gathered.astype(jnp.float32)
    row_mean = jnp.mean(widened, axis=1, keepdims=True)
    centered = widened - row_mean
    variance = jnp.mean(centered * centered, axis=1, keepdims=True)
    normed = (centered * lax.rsqrt(variance + 1e-05) * norm_gain).astype(jnp.bfloat16)
    shard_rows = qkv_weight.shape[0]
    merged = jnp.concatenate(
        [
            qkv_weight.reshape(shard_rows, 3 * local_width),
            out_weight,
            prefix_pool.reshape(shard_rows, 2 * local_width),
        ],
        axis=1,
    )
    along_x = lax.axis_size("wx")
    by_x = lax.all_to_all(
        jnp.broadcast_to(merged[None], (along_x,) + merged.shape), "wx", 0, 0, tiled=False
    )
    by_xz = lax.all_gather(by_x, "wz", axis=0, tiled=False)
    merged_whole = jnp.transpose(by_xz, (1, 0, 2, 3)).reshape(-1, merged.shape[1])
    piece_rows = merged_whole[:, : 3 * local_width]
    out_rows = merged_whole[:, 3 * local_width : 4 * local_width]
    prefix_whole = merged_whole[:, 4 * local_width :]
    piece_count = piece_rows.shape[0]
    columns = normed
    projected = jnp.dot(
        columns,
        piece_rows.reshape(piece_count, 3 * local_width),
        preferred_element_type=jnp.float32,
    )
    projected = projected.reshape(span_rows, 3, heads_here, HEAD_DIM)
    length = cache_len[0]
    offset = jnp.arange(span_rows, dtype=jnp.int32)
    positions = PPAGES * PAGE + length + offset
    queries = rotary(projected[:, 0], positions).astype(jnp.bfloat16)
    keys = rotary(projected[:, 1], positions).astype(jnp.bfloat16)
    values = projected[:, 2].astype(jnp.bfloat16)
    new_pages = jnp.stack(
        [keys.reshape(span_rows, local_width), values.reshape(span_rows, local_width)], axis=1
    )
    initial = (
        jnp.full((heads_here, span_rows), NEGATIVE, jnp.float32),
        jnp.zeros((heads_here, span_rows), jnp.float32),
        jnp.zeros((span_rows, heads_here, HEAD_DIM), jnp.float32),
    )
    running = attend(initial, queries, keys, values, offset[:, None] >= offset[None, :])
    my_group = group_ids[0]
    prefix_pages = prefix_whole.reshape(-1, PAGE, 2, heads_here, HEAD_DIM)
    chosen = lax.dynamic_slice_in_dim(group_pages, my_group * PPAGES, PPAGES)
    key_rows = jnp.take(prefix_pages, chosen, axis=0).reshape(
        PPAGES * PAGE, 2, heads_here, HEAD_DIM
    )
    running = attend(
        running,
        queries,
        key_rows[:, 0],
        key_rows[:, 1],
        jnp.ones((span_rows, PPAGES * PAGE), dtype=bool),
    )
    page_list = page_table[0]
    page_count = cache_pool.shape[0]
    slot_of_page = (
        jnp.zeros((page_count,), jnp.int32)
        .at[page_list]
        .set(jnp.arange(page_count, dtype=jnp.int32))
    )
    block_keys = KB * PAGE
    key_offset = jnp.arange(block_keys, dtype=jnp.int32)

    def cache_block(block_index, state_now):
        key_rows = lax.dynamic_slice_in_dim(cache_pool, block_index * KB, KB, axis=0).reshape(
            block_keys, 2, heads_here, HEAD_DIM
        )
        slots = lax.dynamic_slice_in_dim(slot_of_page, block_index * KB, KB)
        key_slot = jnp.repeat(slots, PAGE) * PAGE + key_offset % PAGE
        key_valid = jnp.broadcast_to((key_slot < length)[None, :], (span_rows, block_keys))
        return attend(state_now, queries, key_rows[:, 0], key_rows[:, 1], key_valid)

    running = lax.fori_loop(0, page_count // KB, cache_block, running)
    head_values = (
        (running[2] / jnp.transpose(running[1])[:, :, None])
        .astype(jnp.bfloat16)
        .reshape(span_rows, local_width)
    )
    all_heads = lax.all_gather(head_values, "narrow", axis=1, tiled=True)
    columns = all_heads
    branch_out = jnp.dot(
        columns,
        out_rows,
        preferred_element_type=jnp.float32,
    )
    return (branch_out.astype(jnp.bfloat16), new_pages)


def split_mesh(mesh):
    grid = mesh.devices
    try:
        along_x = len({device.coords[0] for device in grid[:, 0]})
    except (AttributeError, TypeError):
        along_x = 4
    shape = (along_x, grid.shape[0] // along_x, grid.shape[1])
    return Mesh(grid.reshape(shape), ("wx", "wz", "narrow"))


def solution(mesh):
    W = ("wx", "wz")
    placed = (
        P(W, "narrow"),
        P(),
        P(W, None, "narrow"),
        P(W, "narrow"),
        P(W, None, None, "narrow"),
        P(W, None, "narrow"),
        P(W, None),
        P(W),
        P(W),
        P(),
    )
    return jax.shard_map(
        local,
        mesh=split_mesh(mesh),
        in_specs=placed,
        out_specs=(P(W, "narrow"), P(W, None, "narrow")),
        check_vma=False,
    )
```

```python
import jax
import jax.numpy as jnp
from jax import lax
from jax.sharding import Mesh, PartitionSpec as P

HEAD_DIM = 64
ROT = 16
PAGE = 128
KB = 8
PPAGES = 2


NEGATIVE = -1e30


def rotary(vectors, positions):
    half_rot = ROT // 2
    frequency = 10000.0 ** (-(jnp.arange(half_rot, dtype=jnp.float32) * 2.0 / ROT))
    angles = positions.astype(jnp.float32)[:, None] * frequency[None, :]
    cos_part = jnp.concatenate([jnp.cos(angles), jnp.cos(angles)], axis=1)[:, None, :]
    sine_part = jnp.concatenate([jnp.sin(angles), jnp.sin(angles)], axis=1)[:, None, :]
    rotated_in = vectors[..., :ROT]
    turned = jnp.concatenate([-rotated_in[..., half_rot:], rotated_in[..., :half_rot]], axis=-1)
    return jnp.concatenate(
        [rotated_in * cos_part + turned * sine_part, vectors[..., ROT:]], axis=-1
    )


def attend(running, queries, keys, values, key_valid):
    row_max, weight_sum, weighted = running
    scores = jnp.einsum("qhd,khd->hqk", queries, keys, preferred_element_type=jnp.float32) * 0.125
    scores = jnp.where(key_valid[None], scores, NEGATIVE)
    new_max = jnp.maximum(row_max, jnp.max(scores, axis=2))
    expo = jnp.where(key_valid[None], jnp.exp(scores - new_max[:, :, None]), 0.0)
    factor = jnp.exp(row_max - new_max)
    weight_sum = weight_sum * factor + jnp.sum(expo, axis=2)
    update = jnp.einsum(
        "hqk,khd->qhd", expo.astype(jnp.bfloat16), values, preferred_element_type=jnp.float32
    )
    weighted = weighted * jnp.transpose(factor)[:, :, None] + update
    return (new_max, weight_sum, weighted)


def gather_columns(part):
    count = lax.axis_size("narrow")
    copies = jnp.broadcast_to(part[None], (count,) + part.shape)
    received = lax.all_to_all(copies, "narrow", 0, 0, tiled=False)
    return jnp.transpose(received, (1, 0, 2)).reshape(part.shape[0], count * part.shape[1])


def local(
    tokens,
    norm_gain,
    qkv_weight,
    out_weight,
    cache_pool,
    prefix_pool,
    page_table,
    cache_len,
    group_ids,
    group_pages,
):
    span_rows = tokens.shape[0]
    local_width = qkv_weight.shape[2]
    heads_here = local_width // HEAD_DIM
    gathered = gather_columns(tokens)
    widened = gathered.astype(jnp.float32)
    row_mean = jnp.mean(widened, axis=1, keepdims=True)
    centered = widened - row_mean
    variance = jnp.mean(centered * centered, axis=1, keepdims=True)
    normed = (centered * lax.rsqrt(variance + 1e-05) * norm_gain).astype(jnp.bfloat16)
    shard_rows = qkv_weight.shape[0]
    merged = jnp.concatenate(
        [
            qkv_weight.reshape(shard_rows, 3 * local_width),
            out_weight,
            prefix_pool.reshape(shard_rows, 2 * local_width),
        ],
        axis=1,
    )
    along_x = lax.axis_size("wx")
    by_x = lax.all_to_all(
        jnp.broadcast_to(merged[None], (along_x,) + merged.shape), "wx", 0, 0, tiled=False
    )
    by_xz = lax.all_gather(by_x, "wz", axis=0, tiled=False)
    merged_whole = jnp.transpose(by_xz, (1, 0, 2, 3)).reshape(-1, merged.shape[1])
    piece_rows = merged_whole[:, : 3 * local_width]
    out_rows = merged_whole[:, 3 * local_width : 4 * local_width]
    prefix_whole = merged_whole[:, 4 * local_width :]
    piece_count = piece_rows.shape[0]
    columns = normed
    projected = jnp.dot(
        columns,
        piece_rows.reshape(piece_count, 3 * local_width),
        preferred_element_type=jnp.float32,
    )
    projected = projected.reshape(span_rows, 3, heads_here, HEAD_DIM)
    length = cache_len[0]
    offset = jnp.arange(span_rows, dtype=jnp.int32)
    positions = PPAGES * PAGE + length + offset
    queries = rotary(projected[:, 0], positions).astype(jnp.bfloat16)
    keys = rotary(projected[:, 1], positions).astype(jnp.bfloat16)
    values = projected[:, 2].astype(jnp.bfloat16)
    new_pages = jnp.stack(
        [keys.reshape(span_rows, local_width), values.reshape(span_rows, local_width)], axis=1
    )
    initial = (
        jnp.full((heads_here, span_rows), NEGATIVE, jnp.float32),
        jnp.zeros((heads_here, span_rows), jnp.float32),
        jnp.zeros((span_rows, heads_here, HEAD_DIM), jnp.float32),
    )
    running = attend(initial, queries, keys, values, offset[:, None] >= offset[None, :])
    my_group = group_ids[0]
    chosen = lax.dynamic_slice_in_dim(group_pages, my_group * PPAGES, PPAGES)
    key_rows = jnp.concatenate(
        [lax.dynamic_slice_in_dim(prefix_whole, chosen[k] * PAGE, PAGE, axis=0) for k in range(PPAGES)],
        axis=0,
    ).reshape(PPAGES * PAGE, 2, heads_here, HEAD_DIM)
    running = attend(
        running,
        queries,
        key_rows[:, 0],
        key_rows[:, 1],
        jnp.ones((span_rows, PPAGES * PAGE), dtype=bool),
    )
    page_list = page_table[0]
    page_count = cache_pool.shape[0]
    slot_of_page = (
        jnp.zeros((page_count,), jnp.int32)
        .at[page_list]
        .set(jnp.arange(page_count, dtype=jnp.int32))
    )
    block_keys = KB * PAGE
    key_offset = jnp.arange(block_keys, dtype=jnp.int32)

    def cache_block(block_index, state_now):
        key_rows = lax.dynamic_slice_in_dim(cache_pool, block_index * KB, KB, axis=0).reshape(
            block_keys, 2, heads_here, HEAD_DIM
        )
        slots = lax.dynamic_slice_in_dim(slot_of_page, block_index * KB, KB)
        key_slot = jnp.repeat(slots, PAGE) * PAGE + key_offset % PAGE
        key_valid = jnp.broadcast_to((key_slot < length)[None, :], (span_rows, block_keys))
        return attend(state_now, queries, key_rows[:, 0], key_rows[:, 1], key_valid)

    running = lax.fori_loop(0, page_count // KB, cache_block, running)
    head_values = (
        (running[2] / jnp.transpose(running[1])[:, :, None])
        .astype(jnp.bfloat16)
        .reshape(span_rows, local_width)
    )
    all_heads = lax.all_gather(head_values, "narrow", axis=1, tiled=True)
    columns = all_heads
    branch_out = jnp.dot(
        columns,
        out_rows,
        preferred_element_type=jnp.float32,
    )
    return (branch_out.astype(jnp.bfloat16), new_pages)


def split_mesh(mesh):
    grid = mesh.devices
    try:
        along_x = len({device.coords[0] for device in grid[:, 0]})
    except (AttributeError, TypeError):
        along_x = 4
    shape = (along_x, grid.shape[0] // along_x, grid.shape[1])
    return Mesh(grid.reshape(shape), ("wx", "wz", "narrow"))


def solution(mesh):
    W = ("wx", "wz")
    placed = (
        P(W, "narrow"),
        P(),
        P(W, None, "narrow"),
        P(W, "narrow"),
        P(W, None, None, "narrow"),
        P(W, None, "narrow"),
        P(W, None),
        P(W),
        P(W),
        P(),
    )
    return jax.shard_map(
        local,
        mesh=split_mesh(mesh),
        in_specs=placed,
        out_specs=(P(W, "narrow"), P(W, None, "narrow")),
        check_vma=False,
    )
```

```python
import jax
import jax.numpy as jnp
from jax import lax
from jax.sharding import Mesh, PartitionSpec as P

HEAD_DIM = 64
ROT = 16
PAGE = 128
KB = 12
PPAGES = 2


NEGATIVE = -1e30


def rotary(vectors, positions):
    half_rot = ROT // 2
    frequency = 10000.0 ** (-(jnp.arange(half_rot, dtype=jnp.float32) * 2.0 / ROT))
    angles = positions.astype(jnp.float32)[:, None] * frequency[None, :]
    cos_part = jnp.concatenate([jnp.cos(angles), jnp.cos(angles)], axis=1)[:, None, :]
    sine_part = jnp.concatenate([jnp.sin(angles), jnp.sin(angles)], axis=1)[:, None, :]
    rotated_in = vectors[..., :ROT]
    turned = jnp.concatenate([-rotated_in[..., half_rot:], rotated_in[..., :half_rot]], axis=-1)
    return jnp.concatenate(
        [rotated_in * cos_part + turned * sine_part, vectors[..., ROT:]], axis=-1
    )


def attend(running, queries, keys, values, key_valid):
    row_max, weight_sum, weighted = running
    scores = jnp.einsum("qhd,khd->hqk", queries, keys, preferred_element_type=jnp.float32) * 0.125
    scores = jnp.where(key_valid[None], scores, NEGATIVE)
    new_max = jnp.maximum(row_max, jnp.max(scores, axis=2))
    expo = jnp.where(key_valid[None], jnp.exp(scores - new_max[:, :, None]), 0.0)
    factor = jnp.exp(row_max - new_max)
    weight_sum = weight_sum * factor + jnp.sum(expo, axis=2)
    update = jnp.einsum(
        "hqk,khd->qhd", expo.astype(jnp.bfloat16), values, preferred_element_type=jnp.float32
    )
    weighted = weighted * jnp.transpose(factor)[:, :, None] + update
    return (new_max, weight_sum, weighted)


def gather_columns(part):
    count = lax.axis_size("narrow")
    copies = jnp.broadcast_to(part[None], (count,) + part.shape)
    received = lax.all_to_all(copies, "narrow", 0, 0, tiled=False)
    return jnp.transpose(received, (1, 0, 2)).reshape(part.shape[0], count * part.shape[1])


def local(
    tokens,
    norm_gain,
    qkv_weight,
    out_weight,
    cache_pool,
    prefix_pool,
    page_table,
    cache_len,
    group_ids,
    group_pages,
):
    span_rows = tokens.shape[0]
    local_width = qkv_weight.shape[2]
    heads_here = local_width // HEAD_DIM
    gathered = gather_columns(tokens)
    widened = gathered.astype(jnp.float32)
    row_mean = jnp.mean(widened, axis=1, keepdims=True)
    centered = widened - row_mean
    variance = jnp.mean(centered * centered, axis=1, keepdims=True)
    normed = (centered * lax.rsqrt(variance + 1e-05) * norm_gain).astype(jnp.bfloat16)
    shard_rows = qkv_weight.shape[0]
    merged = jnp.concatenate(
        [
            qkv_weight.reshape(shard_rows, 3 * local_width),
            out_weight,
            prefix_pool.reshape(shard_rows, 2 * local_width),
        ],
        axis=1,
    )
    along_x = lax.axis_size("wx")
    by_x = lax.all_to_all(
        jnp.broadcast_to(merged[None], (along_x,) + merged.shape), "wx", 0, 0, tiled=False
    )
    by_xz = lax.all_gather(by_x, "wz", axis=0, tiled=False)
    merged_whole = jnp.transpose(by_xz, (1, 0, 2, 3)).reshape(-1, merged.shape[1])
    piece_rows = merged_whole[:, : 3 * local_width]
    out_rows = merged_whole[:, 3 * local_width : 4 * local_width]
    prefix_whole = merged_whole[:, 4 * local_width :]
    piece_count = piece_rows.shape[0]
    columns = normed
    projected = jnp.dot(
        columns,
        piece_rows.reshape(piece_count, 3 * local_width),
        preferred_element_type=jnp.float32,
    )
    projected = projected.reshape(span_rows, 3, heads_here, HEAD_DIM)
    length = cache_len[0]
    offset = jnp.arange(span_rows, dtype=jnp.int32)
    positions = PPAGES * PAGE + length + offset
    queries = rotary(projected[:, 0], positions).astype(jnp.bfloat16)
    keys = rotary(projected[:, 1], positions).astype(jnp.bfloat16)
    values = projected[:, 2].astype(jnp.bfloat16)
    new_pages = jnp.stack(
        [keys.reshape(span_rows, local_width), values.reshape(span_rows, local_width)], axis=1
    )
    initial = (
        jnp.full((heads_here, span_rows), NEGATIVE, jnp.float32),
        jnp.zeros((heads_here, span_rows), jnp.float32),
        jnp.zeros((span_rows, heads_here, HEAD_DIM), jnp.float32),
    )
    running = attend(initial, queries, keys, values, offset[:, None] >= offset[None, :])
    my_group = group_ids[0]
    chosen = lax.dynamic_slice_in_dim(group_pages, my_group * PPAGES, PPAGES)
    key_rows = jnp.concatenate(
        [lax.dynamic_slice_in_dim(prefix_whole, chosen[k] * PAGE, PAGE, axis=0) for k in range(PPAGES)],
        axis=0,
    ).reshape(PPAGES * PAGE, 2, heads_here, HEAD_DIM)
    running = attend(
        running,
        queries,
        key_rows[:, 0],
        key_rows[:, 1],
        jnp.ones((span_rows, PPAGES * PAGE), dtype=bool),
    )
    page_list = page_table[0]
    page_count = cache_pool.shape[0]
    slot_of_page = (
        jnp.zeros((page_count,), jnp.int32)
        .at[page_list]
        .set(jnp.arange(page_count, dtype=jnp.int32))
    )
    block_keys = KB * PAGE
    key_offset = jnp.arange(block_keys, dtype=jnp.int32)

    def cache_block(block_index, state_now):
        key_rows = lax.dynamic_slice_in_dim(cache_pool, block_index * KB, KB, axis=0).reshape(
            block_keys, 2, heads_here, HEAD_DIM
        )
        slots = lax.dynamic_slice_in_dim(slot_of_page, block_index * KB, KB)
        key_slot = jnp.repeat(slots, PAGE) * PAGE + key_offset % PAGE
        key_valid = jnp.broadcast_to((key_slot < length)[None, :], (span_rows, block_keys))
        return attend(state_now, queries, key_rows[:, 0], key_rows[:, 1], key_valid)

    running = lax.fori_loop(0, page_count // KB, cache_block, running)
    head_values = (
        (running[2] / jnp.transpose(running[1])[:, :, None])
        .astype(jnp.bfloat16)
        .reshape(span_rows, local_width)
    )
    all_heads = lax.all_gather(head_values, "narrow", axis=1, tiled=True)
    columns = all_heads
    branch_out = jnp.dot(
        columns,
        out_rows,
        preferred_element_type=jnp.float32,
    )
    return (branch_out.astype(jnp.bfloat16), new_pages)


def split_mesh(mesh):
    grid = mesh.devices
    try:
        along_x = len({device.coords[0] for device in grid[:, 0]})
    except (AttributeError, TypeError):
        along_x = 4
    shape = (along_x, grid.shape[0] // along_x, grid.shape[1])
    return Mesh(grid.reshape(shape), ("wx", "wz", "narrow"))


def solution(mesh):
    W = ("wx", "wz")
    placed = (
        P(W, "narrow"),
        P(),
        P(W, None, "narrow"),
        P(W, "narrow"),
        P(W, None, None, "narrow"),
        P(W, None, "narrow"),
        P(W, None),
        P(W),
        P(W),
        P(),
    )
    return jax.shard_map(
        local,
        mesh=split_mesh(mesh),
        in_specs=placed,
        out_specs=(P(W, "narrow"), P(W, None, "narrow")),
        check_vma=False,
    )
```

```python
import jax
import jax.numpy as jnp
from jax import lax
from jax.sharding import Mesh, PartitionSpec as P

HEAD_DIM = 64
ROT = 16
PAGE = 128
KB = 6
PPAGES = 2


NEGATIVE = -1e30


def rotary(vectors, positions):
    half_rot = ROT // 2
    frequency = 10000.0 ** (-(jnp.arange(half_rot, dtype=jnp.float32) * 2.0 / ROT))
    angles = positions.astype(jnp.float32)[:, None] * frequency[None, :]
    cos_part = jnp.concatenate([jnp.cos(angles), jnp.cos(angles)], axis=1)[:, None, :]
    sine_part = jnp.concatenate([jnp.sin(angles), jnp.sin(angles)], axis=1)[:, None, :]
    rotated_in = vectors[..., :ROT]
    turned = jnp.concatenate([-rotated_in[..., half_rot:], rotated_in[..., :half_rot]], axis=-1)
    return jnp.concatenate(
        [rotated_in * cos_part + turned * sine_part, vectors[..., ROT:]], axis=-1
    )


def attend(running, queries, keys, values, key_valid):
    row_max, weight_sum, weighted = running
    scores = jnp.einsum("qhd,khd->hqk", queries, keys, preferred_element_type=jnp.float32) * 0.125
    scores = jnp.where(key_valid[None], scores, NEGATIVE)
    new_max = jnp.maximum(row_max, jnp.max(scores, axis=2))
    expo = jnp.where(key_valid[None], jnp.exp(scores - new_max[:, :, None]), 0.0)
    factor = jnp.exp(row_max - new_max)
    weight_sum = weight_sum * factor + jnp.sum(expo, axis=2)
    update = jnp.einsum(
        "hqk,khd->qhd", expo.astype(jnp.bfloat16), values, preferred_element_type=jnp.float32
    )
    weighted = weighted * jnp.transpose(factor)[:, :, None] + update
    return (new_max, weight_sum, weighted)


def gather_columns(part):
    count = lax.axis_size("narrow")
    copies = jnp.broadcast_to(part[None], (count,) + part.shape)
    received = lax.all_to_all(copies, "narrow", 0, 0, tiled=False)
    return jnp.transpose(received, (1, 0, 2)).reshape(part.shape[0], count * part.shape[1])


def local(
    tokens,
    norm_gain,
    qkv_weight,
    out_weight,
    cache_pool,
    prefix_pool,
    page_table,
    cache_len,
    group_ids,
    group_pages,
):
    span_rows = tokens.shape[0]
    local_width = qkv_weight.shape[2]
    heads_here = local_width // HEAD_DIM
    gathered = gather_columns(tokens)
    widened = gathered.astype(jnp.float32)
    row_mean = jnp.mean(widened, axis=1, keepdims=True)
    centered = widened - row_mean
    variance = jnp.mean(centered * centered, axis=1, keepdims=True)
    normed = (centered * lax.rsqrt(variance + 1e-05) * norm_gain).astype(jnp.bfloat16)
    shard_rows = qkv_weight.shape[0]
    merged = jnp.concatenate(
        [
            qkv_weight.reshape(shard_rows, 3 * local_width),
            out_weight,
            prefix_pool.reshape(shard_rows, 2 * local_width),
        ],
        axis=1,
    )
    along_x = lax.axis_size("wx")
    by_x = lax.all_to_all(
        jnp.broadcast_to(merged[None], (along_x,) + merged.shape), "wx", 0, 0, tiled=False
    )
    by_xz = lax.all_gather(by_x, "wz", axis=0, tiled=False)
    merged_whole = jnp.transpose(by_xz, (1, 0, 2, 3)).reshape(-1, merged.shape[1])
    piece_rows = merged_whole[:, : 3 * local_width]
    out_rows = merged_whole[:, 3 * local_width : 4 * local_width]
    prefix_whole = merged_whole[:, 4 * local_width :]
    piece_count = piece_rows.shape[0]
    columns = normed
    projected = jnp.dot(
        columns,
        piece_rows.reshape(piece_count, 3 * local_width),
        preferred_element_type=jnp.float32,
    )
    projected = projected.reshape(span_rows, 3, heads_here, HEAD_DIM)
    length = cache_len[0]
    offset = jnp.arange(span_rows, dtype=jnp.int32)
    positions = PPAGES * PAGE + length + offset
    queries = rotary(projected[:, 0], positions).astype(jnp.bfloat16)
    keys = rotary(projected[:, 1], positions).astype(jnp.bfloat16)
    values = projected[:, 2].astype(jnp.bfloat16)
    new_pages = jnp.stack(
        [keys.reshape(span_rows, local_width), values.reshape(span_rows, local_width)], axis=1
    )
    initial = (
        jnp.full((heads_here, span_rows), NEGATIVE, jnp.float32),
        jnp.zeros((heads_here, span_rows), jnp.float32),
        jnp.zeros((span_rows, heads_here, HEAD_DIM), jnp.float32),
    )
    running = attend(initial, queries, keys, values, offset[:, None] >= offset[None, :])
    my_group = group_ids[0]
    chosen = lax.dynamic_slice_in_dim(group_pages, my_group * PPAGES, PPAGES)
    key_rows = jnp.concatenate(
        [lax.dynamic_slice_in_dim(prefix_whole, chosen[k] * PAGE, PAGE, axis=0) for k in range(PPAGES)],
        axis=0,
    ).reshape(PPAGES * PAGE, 2, heads_here, HEAD_DIM)
    running = attend(
        running,
        queries,
        key_rows[:, 0],
        key_rows[:, 1],
        jnp.ones((span_rows, PPAGES * PAGE), dtype=bool),
    )
    page_list = page_table[0]
    page_count = cache_pool.shape[0]
    slot_of_page = (
        jnp.zeros((page_count,), jnp.int32)
        .at[page_list]
        .set(jnp.arange(page_count, dtype=jnp.int32))
    )
    block_keys = KB * PAGE
    key_offset = jnp.arange(block_keys, dtype=jnp.int32)

    def cache_block(block_index, state_now):
        key_rows = lax.dynamic_slice_in_dim(cache_pool, block_index * KB, KB, axis=0).reshape(
            block_keys, 2, heads_here, HEAD_DIM
        )
        slots = lax.dynamic_slice_in_dim(slot_of_page, block_index * KB, KB)
        key_slot = jnp.repeat(slots, PAGE) * PAGE + key_offset % PAGE
        key_valid = jnp.broadcast_to((key_slot < length)[None, :], (span_rows, block_keys))
        return attend(state_now, queries, key_rows[:, 0], key_rows[:, 1], key_valid)

    running = lax.fori_loop(0, page_count // KB, cache_block, running)
    head_values = (
        (running[2] / jnp.transpose(running[1])[:, :, None])
        .astype(jnp.bfloat16)
        .reshape(span_rows, local_width)
    )
    all_heads = lax.all_gather(head_values, "narrow", axis=1, tiled=True)
    columns = all_heads
    branch_out = jnp.dot(
        columns,
        out_rows,
        preferred_element_type=jnp.float32,
    )
    return (branch_out.astype(jnp.bfloat16), new_pages)


def split_mesh(mesh):
    grid = mesh.devices
    try:
        along_x = len({device.coords[0] for device in grid[:, 0]})
    except (AttributeError, TypeError):
        along_x = 4
    shape = (along_x, grid.shape[0] // along_x, grid.shape[1])
    return Mesh(grid.reshape(shape), ("wx", "wz", "narrow"))


def solution(mesh):
    W = ("wx", "wz")
    placed = (
        P(W, "narrow"),
        P(),
        P(W, None, "narrow"),
        P(W, "narrow"),
        P(W, None, None, "narrow"),
        P(W, None, "narrow"),
        P(W, None),
        P(W),
        P(W),
        P(),
    )
    return jax.shard_map(
        local,
        mesh=split_mesh(mesh),
        in_specs=placed,
        out_specs=(P(W, "narrow"), P(W, None, "narrow")),
        check_vma=False,
    )
```
